1024 devices in a mesh: pipe: 16 (over y, core), seq: 16 (over z), tp: 4 (over x).
Axes of the slice: x: 4, y: 8, z: 16, core: 2. Of those that a mesh axis runs over, the one named last changes fastest.
Arguments:
- emitted: bfloat16 [16, 2048, 8192], P('pipe', 'seq', 'tp'), may hold values from -6 to 6
- cotangent: bfloat16 [16, 2048, 8192], P('pipe', 'seq', 'tp'), may hold values from -6 to 6
- b_proj: bfloat16 [16, 2048, 512], P('pipe', 'seq', 'tp'), may hold values from -0.26367188 to 0.26367188
- c_proj: bfloat16 [16, 2048, 512], P('pipe', 'seq', 'tp'), may hold values from -0.52734375 to 0.52734375
- log_decay: bfloat16 [16, 2048, 128], P('pipe', 'seq', 'tp'), may hold values from -1 to 0
- starts: int32 [16, 2048], P('pipe', 'seq'), may hold values 0 or 1
- skip: float32 [16, 128], P('pipe', 'tp'), may hold values from 0.5 to 2
Outputs:
- mixed: bfloat16 [16, 2048, 8192], P('pipe', 'seq', 'tp')
- input_grad: bfloat16 [16, 2048, 8192], P('pipe', 'seq', 'tp')
The draws below stay inside these ranges and needn't reach their ends.
All inputs are finite; a program needn't handle non-finite values. No bound on the sum of `starts` on one device may be relied on, other than what follows from the above.
Results may differ from the reference program's by a relative error of at most 0.001.
Values may be sent and summed in bfloat16 or wider, within the bound.
No kernel may reach another device: no remote copies, remote signals or barrier semaphores. Data moves between devices by JAX's collectives and lax.ppermute only.
A program may use at most 32 MiB of HBM per device.

```python
import math
import jax
import jax.numpy as jnp
from jax import lax

TOK_DEV = 128
BLEND_CHANNELS = 128
P_SIZE = 64
N = 128
GROUPS = 4
SPAN = 128
EPISODE_STEPS = 2048
HANDOFF_PARTS = 16


def draw_log_decay(key, part):
    stochastic_seeds = jax.random.split(key, 7)
    quick_heads = jax.random.randint(stochastic_seeds[0], (HANDOFF_PARTS, 1, BLEND_CHANNELS), 0, 2) == 0
    quick_rate = jnp.exp(jax.random.uniform(stochastic_seeds[1], (HANDOFF_PARTS, 1, BLEND_CHANNELS), jnp.float32, math.log(1.0 / 50.0), math.log(1.0 / 30.0)))
    slow_rate = jnp.exp(jax.random.uniform(stochastic_seeds[2], (HANDOFF_PARTS, 1, BLEND_CHANNELS), jnp.float32, math.log(0.05), math.log(0.3))) / EPISODE_STEPS
    background_intensity = jnp.where(quick_heads, quick_rate, slow_rate)
    shards = EPISODE_STEPS // TOK_DEV
    partition_scaling = jnp.exp(jax.random.uniform(stochastic_seeds[3], (HANDOFF_PARTS, shards, 1, BLEND_CHANNELS), jnp.float32, 0.0, math.log(3.0)))
    partition_scaling = jnp.broadcast_to(partition_scaling, (HANDOFF_PARTS, shards, TOK_DEV, BLEND_CHANNELS)).reshape(HANDOFF_PARTS, EPISODE_STEPS, BLEND_CHANNELS)
    element_scaling = jax.random.uniform(stochastic_seeds[4], (HANDOFF_PARTS, EPISODE_STEPS, BLEND_CHANNELS), jnp.float32, 0.5, 1.5)
    spike_locations = jax.random.randint(stochastic_seeds[5], (HANDOFF_PARTS, 2, BLEND_CHANNELS), 0, EPISODE_STEPS)
    spike_amplitudes = jnp.exp(jax.random.uniform(stochastic_seeds[6], (HANDOFF_PARTS, 2, BLEND_CHANNELS), jnp.float32, math.log(0.22), math.log(0.69)))
    location_table = jnp.arange(EPISODE_STEPS)[None, :, None]
    spike_occurrences = (location_table == spike_locations[:, 0:1, :]) * spike_amplitudes[:, 0:1, :] + (location_table == spike_locations[:, 1:2, :]) * spike_amplitudes[:, 1:2, :]
    combined = -(background_intensity * partition_scaling * element_scaling) - spike_occurrences
    return jnp.maximum(combined, -0.99).astype(jnp.bfloat16)


def touch_ends(array, own_key, low, largest):
    place = [jax.random.randint(jax.random.fold_in(own_key, axis), (), 0, length) for axis, length in enumerate(array.shape)]
    widest = array.shape.index(max(array.shape))
    neighbour = place[:widest] + [(place[widest] + 1) % array.shape[widest]] + place[widest + 1:]
    return array.at[tuple(place)].set(low).at[tuple(neighbour)].set(largest)


def steps_of(stream_key, dims, cuts, smallest, high):
    def one(dim, parts):
        heights = jax.random.uniform(jax.random.fold_in(jax.random.fold_in(stream_key, 6), dim), (parts,), jnp.float32, smallest / len(cuts), high / len(cuts))
        return jnp.repeat(jnp.exp(heights), dims[dim] // parts).reshape((-1,) + (1,) * (len(dims) - dim - 1))

    loudness = one(*cuts[0])
    for cut in cuts[1:]:
        loudness = loudness * one(*cut)
    return loudness


def bell_draw(key, shape, scale, bound, cuts=(), dtype=jnp.bfloat16):
    values = jax.random.normal(key, shape, jnp.float32) * scale
    if len(cuts) > 0:
        values = steps_of(key, shape, cuts, -0.22, 0.18) * values
    return jnp.clip(values, min=-bound, max=bound).astype(dtype)


def setup_inputs(seed: int = 0) -> dict:
    key_list = jax.random.split(jax.random.key(seed), 8)
    emitted = bell_draw(key_list[0], (HANDOFF_PARTS, EPISODE_STEPS, BLEND_CHANNELS * P_SIZE), 1.0, 6.0, ((0, 16), (1, 16), (2, 4)))
    cotangent = bell_draw(key_list[1], (HANDOFF_PARTS, EPISODE_STEPS, BLEND_CHANNELS * P_SIZE), 1.0, 6.0, ((0, 16), (1, 16), (2, 4)))
    b_proj = bell_draw(key_list[2], (HANDOFF_PARTS, EPISODE_STEPS, GROUPS * N), (0.5 * N ** -0.5), 0.26367188, ((0, 16), (1, 16), (2, 4)))
    c_proj = bell_draw(key_list[3], (HANDOFF_PARTS, EPISODE_STEPS, GROUPS * N), (N ** -0.5), 0.52734375, ((0, 16), (1, 16), (2, 4)))
    log_decay = draw_log_decay(jax.random.fold_in(key_list[7], 71), 0)
    starts = touch_ends((jax.random.randint(key_list[5], (HANDOFF_PARTS, EPISODE_STEPS), 0, 4 * TOK_DEV) < 1).astype(jnp.int32), jax.random.fold_in(key_list[5], 1), 0, 1)
    skip = jnp.clip(jnp.exp(math.log(2.0) - 1.3862944 * jax.random.uniform(key_list[6], (HANDOFF_PARTS, BLEND_CHANNELS), jnp.float32) ** steps_of(key_list[6], (HANDOFF_PARTS, BLEND_CHANNELS), ((0, 16), (1, 4)), -0.2, 0.2)), 0.5, 2.0)
    return {"emitted": emitted, "cotangent": cotangent, "b_proj": b_proj, "c_proj": c_proj, "log_decay": log_decay, "starts": starts, "skip": skip}


HIGH = lax.Precision.HIGHEST


def single_terms(inputs, upstream, b_rows, c_rows, decay_rows, opened):
    running = jnp.cumsum(decay_rows, axis=1)
    running_end = running[:, -1]
    opened_sum = jnp.cumsum(opened, axis=1)
    opened_end = opened_sum[:, -1]
    width = inputs.shape[1]
    causal = jnp.arange(width)[:, None] >= jnp.arange(width)[None, :]
    linked = (opened_sum[:, :, None] == opened_sum[:, None, :]) & causal[None]
    spread = running[:, :, None] - running[:, None, :]
    damping = jnp.where(linked[:, :, :, None, None], jnp.exp(jnp.minimum(spread, 0.0)), 0.0)
    intersection = jnp.einsum("ktgn,ksgn->ktsg", c_rows, b_rows, precision=HIGH)
    mixing = damping * intersection[..., None]
    mixed_part = jnp.einsum("ktsge,ksgep->ktgep", mixing, inputs, precision=HIGH)
    grad_part = jnp.einsum("ktsge,ktgep->ksgep", mixing, upstream, precision=HIGH)
    inflow = jnp.exp(running) * (opened_sum == 0.0)[:, :, None, None]
    outflow = jnp.exp(running_end[:, None] - running) * (opened_sum == opened_end[:, None])[:, :, None, None]
    through = jnp.exp(running_end) * (opened_end == 0.0)[:, None, None]
    end_states = jnp.einsum("ksgn,ksgep->kgenp", b_rows, inputs * outflow[..., None], precision=HIGH)
    start_states = jnp.einsum("ksgn,ksgep->kgenp", c_rows, upstream * inflow[..., None], precision=HIGH)
    return mixed_part, grad_part, inflow, outflow, through, end_states, start_states


def block_terms(inputs, upstream, b_rows, c_rows, decay_rows, opened):
    def one_block(pieces):
        result = single_terms(*[piece[None] for piece in pieces])
        return tuple(item[0] for item in result)
    return lax.map(one_block, (inputs, upstream, b_rows, c_rows, decay_rows, opened))


def pass_forward(through, end_states, first_state):
    def advance(current, element):
        return element[0][:, :, None, None] * current + element[1], current
    final, entering = lax.scan(advance, first_state, (through, end_states))
    return entering, final


def pass_backward(through, start_states, last_state):
    def advance(current, element):
        return element[0][:, :, None, None] * current + element[1], current
    final, leaving = lax.scan(advance, last_state, (through, start_states), reverse=True)
    return leaving, final


def finish(terms, inputs, upstream, b_rows, c_rows, skip_gain, first_state, last_state):
    mixed_part, grad_part, inflow, outflow, through, end_states, start_states = terms
    entering, _ = pass_forward(through, end_states, first_state)
    leaving, _ = pass_backward(through, start_states, last_state)
    gain_wide = skip_gain[None, None, :, :, None]
    mixed = mixed_part + jnp.einsum("ktgn,kgenp->ktgep", c_rows, entering, precision=HIGH) * inflow[..., None] + gain_wide * inputs
    grads = grad_part + jnp.einsum("ktgn,kgenp->ktgep", b_rows, leaving, precision=HIGH) * outflow[..., None] + gain_wide * upstream
    return mixed, grads


def section(pieces):
    inputs, upstream, b_proj, c_proj, log_decay, starts, skip = pieces
    block_count = EPISODE_STEPS // SPAN
    per_group = BLEND_CHANNELS // GROUPS
    blocked = (block_count, SPAN, GROUPS, per_group, P_SIZE)
    values = inputs.astype(jnp.float32).reshape(blocked)
    grads_in = upstream.astype(jnp.float32).reshape(blocked)
    b_rows = b_proj.astype(jnp.float32).reshape(block_count, SPAN, GROUPS, N)
    c_rows = c_proj.astype(jnp.float32).reshape(block_count, SPAN, GROUPS, N)
    decay_rows = log_decay.astype(jnp.float32).reshape(block_count, SPAN, GROUPS, per_group)
    opened = starts.astype(jnp.float32).reshape(block_count, SPAN)
    skip_gain = skip.reshape(GROUPS, per_group)
    terms = block_terms(values, grads_in, b_rows, c_rows, decay_rows, opened)
    empty_state = jnp.zeros((GROUPS, per_group, N, P_SIZE), jnp.float32)
    mixed, grads = finish(terms, values, grads_in, b_rows, c_rows, skip_gain, empty_state, empty_state)
    return (mixed.reshape(EPISODE_STEPS, BLEND_CHANNELS * P_SIZE).astype(jnp.bfloat16), grads.reshape(EPISODE_STEPS, BLEND_CHANNELS * P_SIZE).astype(jnp.bfloat16))


def reference(emitted, cotangent, b_proj, c_proj, log_decay, starts, skip):
    inputs = jnp.concatenate([emitted[:1], emitted[:-1]], axis=0)
    mixed, input_grad = lax.map(section, (inputs, cotangent, b_proj, c_proj, log_decay, starts, skip))
    return mixed, input_grad
```

```python
import jax
import jax.numpy as jnp
from jax import lax
from jax.sharding import PartitionSpec as P

BLEND_CHANNELS = 128
P_SIZE = 64
N = 128
GROUPS = 4
MISC = 16

F32 = jnp.float32
BF16 = jnp.bfloat16
HIGH = lax.Precision.HIGHEST


def from_behind(value, axis, steps):
    count = lax.axis_size(axis)
    leading, last = (max(0, -steps), min(count, count - steps))
    return lax.ppermute(value, axis, [(source, source + steps) for source in range(leading, last)])


def mm(spec, a, b):
    return jnp.einsum(spec, a, b, preferred_element_type=F32)


def mm_wide(spec, a, b):
    return jnp.einsum(spec, a.astype(F32), b.astype(F32), precision=HIGH)


mm_right = mm_wide
mm_left = mm_wide


def mix(xk, gk, bk, ck, deck, flk, gain):
    chunks, width = flk.shape
    order = jnp.arange(width)
    causal = order[:, None] >= order[None, :]
    tri = causal.astype(BF16)
    cum = mm("tu,khu->kht", tri, deck)
    seg = mm("tu,ku->kt", tri, flk)
    linked = (seg[:, :, None] == seg[:, None, :]) & causal[None]
    spread = cum[:, :, :, None] - cum[:, :, None, :]
    damping = jnp.where(linked[:, None], jnp.exp(jnp.minimum(spread, 0.0)), 0.0)
    overlap = mm("ktn,kun->ktu", ck, bk)
    mixing = damping * overlap[:, None]
    mixed = mm_left("khtu,kuhp->kthp", mixing, xk)
    grads = mm_left("khtu,kthp->kuhp", mixing, gk)

    cum_end = cum[:, :, -1]
    seg_end = seg[:, -1]
    outflow = jnp.exp(cum_end[:, :, None] - cum) * (seg == seg_end[:, None])[:, None, :]
    inflow = jnp.exp(cum) * (seg == 0.0)[:, None, :]
    outflow_q = outflow.transpose(0, 2, 1)[..., None]
    inflow_q = inflow.transpose(0, 2, 1)[..., None]
    end_states = mm_right("kun,kuhp->khnp", bk, outflow_q * xk.astype(F32))
    start_states = mm_right("ktn,kthp->khnp", ck, inflow_q * gk.astype(F32))

    total = jnp.cumsum(cum_end, axis=0)
    opened = jnp.cumsum((seg_end > 0.0).astype(F32))
    total_prev = jnp.concatenate([jnp.zeros_like(total[:1]), total[:-1]], axis=0)
    opened_prev = jnp.concatenate([jnp.zeros_like(opened[:1]), opened[:-1]], axis=0)
    index = jnp.arange(chunks)
    reach = (index[None, :] < index[:, None]) & (opened_prev[:, None] == opened[None, :])
    carry = jnp.where(
        reach[:, :, None],
        jnp.exp(jnp.minimum(total_prev[:, None, :] - total[None, :, :], 0.0)),
        0.0,
    )
    entering = jnp.einsum("kjh,jhnp->khnp", carry, end_states, precision=HIGH)
    leaving = jnp.einsum("jkh,jhnp->khnp", carry, start_states, precision=HIGH)

    mixed = mixed + inflow_q * mm_right("ktn,khnp->kthp", ck, entering)
    grads = grads + outflow_q * mm_right("kun,khnp->kuhp", bk, leaving)
    gain_wide = gain[None, None, :, None]
    mixed = mixed + gain_wide * xk.astype(F32)
    grads = grads + gain_wide * gk.astype(F32)
    return mixed, grads


def body(emitted, cotangent, b_proj, c_proj, log_decay, starts, skip):
    shifted = from_behind(emitted, "pipe", 1)
    inputs = jnp.where(lax.axis_index("pipe") == 0, emitted, shifted)[0]
    upstream = cotangent[0]
    length_dev = inputs.shape[0]
    seq_count = lax.axis_size("seq")
    local_heads = skip.shape[1]
    head_share = local_heads // seq_count
    lanes = head_share * P_SIZE
    per_group = BLEND_CHANNELS // GROUPS
    position = lax.axis_index("seq")
    first_head = position * head_share
    group_pick = first_head // per_group
    group_count = b_proj.shape[2] // N

    decay_rows = log_decay[0].reshape(length_dev, seq_count, head_share).transpose(1, 2, 0)
    flag_rows = jnp.broadcast_to(
        starts[0].astype(BF16)[None, None, :], (seq_count, 1, length_dev)
    )
    filler = jnp.zeros((seq_count, MISC - head_share - 1, length_dev), BF16)
    payload = jnp.concatenate(
        [
            inputs.reshape(length_dev, seq_count, lanes).transpose(1, 0, 2),
            upstream.reshape(length_dev, seq_count, lanes).transpose(1, 0, 2),
            decay_rows,
            flag_rows,
            filler,
        ],
        axis=1,
    )
    got = lax.all_to_all(payload, "seq", split_axis=0, concat_axis=0, tiled=True)

    proj = jnp.concatenate([b_proj[0], c_proj[0]], axis=-1)
    proj_whole = lax.all_gather(proj, "seq", axis=0, tiled=True)
    proj_whole = proj_whole.reshape(seq_count, length_dev, 2, group_count, N)
    proj_pick = lax.dynamic_index_in_dim(proj_whole, group_pick, axis=3, keepdims=False)
    bk = proj_pick[:, :, 0]
    ck = proj_pick[:, :, 1]

    xk = got[:, :length_dev].reshape(seq_count, length_dev, head_share, P_SIZE)
    gk = got[:, length_dev : 2 * length_dev].reshape(seq_count, length_dev, head_share, P_SIZE)
    deck = got[:, 2 * length_dev : 2 * length_dev + head_share]
    flk = got[:, 2 * length_dev + head_share]
    gain = lax.dynamic_slice_in_dim(skip[0], first_head, head_share)

    mixed, grads = mix(xk, gk, bk, ck, deck, flk, gain)
    homeward = jnp.concatenate(
        [
            mixed.reshape(seq_count, length_dev, lanes),
            grads.reshape(seq_count, length_dev, lanes),
        ],
        axis=1,
    ).astype(BF16)
    back = lax.all_to_all(homeward, "seq", split_axis=0, concat_axis=0, tiled=True)
    mixed_out = back[:, :length_dev].transpose(1, 0, 2).reshape(1, length_dev, local_heads * P_SIZE)
    grad_out = back[:, length_dev:].transpose(1, 0, 2).reshape(1, length_dev, local_heads * P_SIZE)
    return (mixed_out, grad_out)


def solution(mesh):
    placed = (
        P("pipe", "seq", "tp"),
        P("pipe", "seq", "tp"),
        P("pipe", "seq", "tp"),
        P("pipe", "seq", "tp"),
        P("pipe", "seq", "tp"),
        P("pipe", "seq"),
        P("pipe", "tp"),
    )
    return jax.shard_map(
        body,
        mesh=mesh,
        in_specs=placed,
        out_specs=(P("pipe", "seq", "tp"), P("pipe", "seq", "tp")),
        check_vma=False,
    )
```

```python
import jax
import jax.numpy as jnp
from jax import lax
from jax.sharding import PartitionSpec as P

BLEND_CHANNELS = 128
P_SIZE = 64
N = 128
GROUPS = 4
MISC = 16

F32 = jnp.float32
BF16 = jnp.bfloat16
HIGH = lax.Precision.HIGHEST


def from_behind(value, axis, steps):
    count = lax.axis_size(axis)
    leading, last = (max(0, -steps), min(count, count - steps))
    return lax.ppermute(value, axis, [(source, source + steps) for source in range(leading, last)])


def ring_shift(value, axis, steps):
    count = lax.axis_size(axis)
    return lax.ppermute(value, axis, [(source, (source + steps) % count) for source in range(count)])


def ring_gather(block, axis, position):
    count = lax.axis_size(axis)
    ahead = count // 2
    behind = count - 1 - ahead
    from_left = [block]
    from_right = [block]
    for _ in range(ahead):
        from_left.append(ring_shift(from_left[-1], axis, 1))
    for _ in range(behind):
        from_right.append(ring_shift(from_right[-1], axis, -1))
    relative = [block] + from_right[1:] + from_left[1:][::-1]
    stacked = jnp.stack(relative + relative, axis=0)
    return lax.dynamic_slice_in_dim(stacked, (count - position) % count, count, axis=0)


def mm(spec, a, b):
    return jnp.einsum(spec, a, b, preferred_element_type=F32)


def mm_wide(spec, a, b):
    return jnp.einsum(spec, a.astype(F32), b.astype(F32), precision=HIGH)


mm_right = mm_wide
mm_left = mm_wide


def mix(xk, gk, bk, ck, deck, flk, gain):
    chunks, width = flk.shape
    order = jnp.arange(width)
    causal = order[:, None] >= order[None, :]
    tri = causal.astype(BF16)
    cum = mm("tu,khu->kht", tri, deck)
    seg = mm("tu,ku->kt", tri, flk)
    linked = (seg[:, :, None] == seg[:, None, :]) & causal[None]
    spread = cum[:, :, :, None] - cum[:, :, None, :]
    damping = jnp.where(linked[:, None], jnp.exp(jnp.minimum(spread, 0.0)), 0.0)
    overlap = mm("ktn,kun->ktu", ck, bk)
    mixing = damping * overlap[:, None]
    mixed = mm_left("khtu,kuhp->kthp", mixing, xk)
    grads = mm_left("khtu,kthp->kuhp", mixing, gk)

    cum_end = cum[:, :, -1]
    seg_end = seg[:, -1]
    outflow = jnp.exp(cum_end[:, :, None] - cum) * (seg == seg_end[:, None])[:, None, :]
    inflow = jnp.exp(cum) * (seg == 0.0)[:, None, :]
    outflow_q = outflow.transpose(0, 2, 1)[..., None]
    inflow_q = inflow.transpose(0, 2, 1)[..., None]
    end_states = mm_right("kun,kuhp->khnp", bk, outflow_q * xk.astype(F32))
    start_states = mm_right("ktn,kthp->khnp", ck, inflow_q * gk.astype(F32))

    total = jnp.cumsum(cum_end, axis=0)
    opened = jnp.cumsum((seg_end > 0.0).astype(F32))
    total_prev = jnp.concatenate([jnp.zeros_like(total[:1]), total[:-1]], axis=0)
    opened_prev = jnp.concatenate([jnp.zeros_like(opened[:1]), opened[:-1]], axis=0)
    index = jnp.arange(chunks)
    reach = (index[None, :] < index[:, None]) & (opened_prev[:, None] == opened[None, :])
    carry = jnp.where(
        reach[:, :, None],
        jnp.exp(jnp.minimum(total_prev[:, None, :] - total[None, :, :], 0.0)),
        0.0,
    )
    entering = jnp.einsum("kjh,jhnp->khnp", carry, end_states, precision=HIGH)
    leaving = jnp.einsum("jkh,jhnp->khnp", carry, start_states, precision=HIGH)

    mixed = mixed + inflow_q * mm_right("ktn,khnp->kthp", ck, entering)
    grads = grads + outflow_q * mm_right("kun,khnp->kuhp", bk, leaving)
    gain_wide = gain[None, None, :, None]
    mixed = mixed + gain_wide * xk.astype(F32)
    grads = grads + gain_wide * gk.astype(F32)
    return mixed, grads


def body(emitted, cotangent, b_proj, c_proj, log_decay, starts, skip):
    shifted = from_behind(emitted, "pipe", 1)
    inputs = jnp.where(lax.axis_index("pipe") == 0, emitted, shifted)[0]
    upstream = cotangent[0]
    length_dev = inputs.shape[0]
    seq_count = lax.axis_size("seq")
    local_heads = skip.shape[1]
    head_share = local_heads // seq_count
    lanes = head_share * P_SIZE
    per_group = BLEND_CHANNELS // GROUPS
    position = lax.axis_index("seq")
    first_head = position * head_share
    group_pick = first_head // per_group
    group_count = b_proj.shape[2] // N

    decay_rows = log_decay[0].reshape(length_dev, seq_count, head_share).transpose(1, 2, 0)
    flag_rows = jnp.broadcast_to(
        starts[0].astype(BF16)[None, None, :], (seq_count, 1, length_dev)
    )
    filler = jnp.zeros((seq_count, MISC - head_share - 1, length_dev), BF16)
    payload = jnp.concatenate(
        [
            inputs.reshape(length_dev, seq_count, lanes).transpose(1, 0, 2),
            upstream.reshape(length_dev, seq_count, lanes).transpose(1, 0, 2),
            decay_rows,
            flag_rows,
            filler,
        ],
        axis=1,
    )
    got = lax.all_to_all(payload, "seq", split_axis=0, concat_axis=0, tiled=True)

    proj = jnp.concatenate([b_proj[0], c_proj[0]], axis=-1)
    proj_whole = ring_gather(proj, "seq", position)
    proj_whole = proj_whole.reshape(seq_count, length_dev, 2, group_count, N)
    proj_pick = lax.dynamic_index_in_dim(proj_whole, group_pick, axis=3, keepdims=False)
    bk = proj_pick[:, :, 0]
    ck = proj_pick[:, :, 1]

    xk = got[:, :length_dev].reshape(seq_count, length_dev, head_share, P_SIZE)
    gk = got[:, length_dev : 2 * length_dev].reshape(seq_count, length_dev, head_share, P_SIZE)
    deck = got[:, 2 * length_dev : 2 * length_dev + head_share]
    flk = got[:, 2 * length_dev + head_share]
    gain = lax.dynamic_slice_in_dim(skip[0], first_head, head_share)

    mixed, grads = mix(xk, gk, bk, ck, deck, flk, gain)
    homeward = jnp.concatenate(
        [
            mixed.reshape(seq_count, length_dev, lanes),
            grads.reshape(seq_count, length_dev, lanes),
        ],
        axis=1,
    ).astype(BF16)
    back = lax.all_to_all(homeward, "seq", split_axis=0, concat_axis=0, tiled=True)
    mixed_out = back[:, :length_dev].transpose(1, 0, 2).reshape(1, length_dev, local_heads * P_SIZE)
    grad_out = back[:, length_dev:].transpose(1, 0, 2).reshape(1, length_dev, local_heads * P_SIZE)
    return (mixed_out, grad_out)


def solution(mesh):
    placed = (
        P("pipe", "seq", "tp"),
        P("pipe", "seq", "tp"),
        P("pipe", "seq", "tp"),
        P("pipe", "seq", "tp"),
        P("pipe", "seq", "tp"),
        P("pipe", "seq"),
        P("pipe", "tp"),
    )
    return jax.shard_map(
        body,
        mesh=mesh,
        in_specs=placed,
        out_specs=(P("pipe", "seq", "tp"), P("pipe", "seq", "tp")),
        check_vma=False,
    )
```

```python
import jax
import jax.numpy as jnp
from jax import lax
from jax.sharding import Mesh
from jax.sharding import PartitionSpec as P

BLEND_CHANNELS = 128
P_SIZE = 64
N = 128
GROUPS = 4
MISC = 16
LOCAL = 4

F32 = jnp.float32
BF16 = jnp.bfloat16
HIGH = lax.Precision.HIGHEST
SEQ = ("hi", "lo")


def from_behind(value, axis, steps):
    count = lax.axis_size(axis)
    leading, last = (max(0, -steps), min(count, count - steps))
    return lax.ppermute(value, axis, [(source, source + steps) for source in range(leading, last)])


def mm(spec, a, b):
    return jnp.einsum(spec, a, b, preferred_element_type=F32)


def mm_wide(spec, a, b):
    return jnp.einsum(spec, a.astype(F32), b.astype(F32), precision=HIGH)


def local_terms(xk, gk, bk, ck, deck, flk):
    chunks, width = flk.shape
    order = jnp.arange(width)
    causal = order[:, None] >= order[None, :]
    tri = causal.astype(BF16)
    cum = mm("tu,khu->kht", tri, deck)
    seg = mm("tu,ku->kt", tri, flk)

    cum_end = cum[:, :, -1]
    seg_end = seg[:, -1]
    outflow = jnp.exp(cum_end[:, :, None] - cum) * (seg == seg_end[:, None])[:, None, :]
    inflow = jnp.exp(cum) * (seg == 0.0)[:, None, :]
    outflow_q = outflow.transpose(0, 2, 1)[..., None]
    inflow_q = inflow.transpose(0, 2, 1)[..., None]
    end_states = mm_wide("kun,kuhp->khnp", bk, outflow_q * xk.astype(F32))
    start_states = mm_wide("ktn,kthp->khnp", ck, inflow_q * gk.astype(F32))

    total = jnp.cumsum(cum_end, axis=0)
    opened = jnp.cumsum((seg_end > 0.0).astype(F32))
    total_prev = jnp.concatenate([jnp.zeros_like(total[:1]), total[:-1]], axis=0)
    opened_prev = jnp.concatenate([jnp.zeros_like(opened[:1]), opened[:-1]], axis=0)
    index = jnp.arange(chunks)
    reach = (index[None, :] < index[:, None]) & (opened_prev[:, None] == opened[None, :])
    carry = jnp.where(
        reach[:, :, None],
        jnp.exp(jnp.minimum(total_prev[:, None, :] - total[None, :, :], 0.0)),
        0.0,
    )
    from_start = jnp.exp(total_prev) * (opened_prev == 0.0)[:, None]
    to_end = jnp.exp(jnp.minimum(total[-1][None, :] - total, 0.0)) * (opened == opened[-1])[:, None]
    through = jnp.exp(total[-1]) * (opened[-1] == 0.0)
    block_end = jnp.einsum("kh,khnp->hnp", to_end, end_states, precision=HIGH)
    block_start = jnp.einsum("kh,khnp->hnp", from_start, start_states, precision=HIGH)
    parts = dict(
        cum=cum, seg=seg, causal=causal, inflow_q=inflow_q, outflow_q=outflow_q,
        end_states=end_states, start_states=start_states, carry=carry,
        from_start=from_start, to_end=to_end,
    )
    return parts, through, block_end, block_start


def finish(parts, xk, gk, bk, ck, gain, entering_block, leaving_block):
    cum, seg, causal = parts["cum"], parts["seg"], parts["causal"]
    linked = (seg[:, :, None] == seg[:, None, :]) & causal[None]
    spread = cum[:, :, :, None] - cum[:, :, None, :]
    damping = jnp.where(linked[:, None], jnp.exp(jnp.minimum(spread, 0.0)), 0.0)
    overlap = mm("ktn,kun->ktu", ck, bk)
    mixing = damping * overlap[:, None]
    mixed = mm_wide("khtu,kuhp->kthp", mixing, xk)
    grads = mm_wide("khtu,kthp->kuhp", mixing, gk)

    carry = parts["carry"]
    entering = jnp.einsum("kjh,jhnp->khnp", carry, parts["end_states"], precision=HIGH)
    leaving = jnp.einsum("jkh,jhnp->khnp", carry, parts["start_states"], precision=HIGH)
    entering = entering + parts["from_start"][:, :, None, None] * entering_block[None]
    leaving = leaving + parts["to_end"][:, :, None, None] * leaving_block[None]

    mixed = mixed + parts["inflow_q"] * mm_wide("ktn,khnp->kthp", ck, entering)
    grads = grads + parts["outflow_q"] * mm_wide("kun,khnp->kuhp", bk, leaving)
    gain_wide = gain[None, None, :, None]
    mixed = mixed + gain_wide * xk.astype(F32)
    grads = grads + gain_wide * gk.astype(F32)
    return mixed, grads


def body(emitted, cotangent, b_proj, c_proj, log_decay, starts, skip):
    shifted = from_behind(emitted, "pipe", 1)
    inputs = jnp.where(lax.axis_index("pipe") == 0, emitted, shifted)[0]
    upstream = cotangent[0]
    length_dev = inputs.shape[0]
    lo_count = lax.axis_size("lo")
    hi_count = lax.axis_size("hi")
    local_heads = skip.shape[1]
    head_share = local_heads // lo_count
    lanes = head_share * P_SIZE
    rows = lanes * length_dev // 128
    lo_pos = lax.axis_index("lo")
    first_head = lo_pos * head_share

    def to_rows(value):
        return value.reshape(length_dev, lo_count, lanes).transpose(1, 0, 2).reshape(lo_count, rows, 128)

    decay_rows = log_decay[0].reshape(length_dev, lo_count, head_share).transpose(1, 2, 0)
    flag_rows = jnp.broadcast_to(starts[0].astype(BF16)[None, None, :], (lo_count, 1, length_dev))
    proj = jnp.concatenate([b_proj[0], c_proj[0]], axis=0)
    proj_rows = jnp.broadcast_to(proj[None], (lo_count,) + proj.shape)
    filler = jnp.zeros((lo_count, MISC - head_share - 1, length_dev), BF16)
    payload = jnp.concatenate(
        [to_rows(inputs), to_rows(upstream), proj_rows, decay_rows, flag_rows, filler], axis=1
    )
    got = lax.all_to_all(payload, "lo", split_axis=0, concat_axis=0, tiled=True)

    xk = got[:, :rows].reshape(lo_count, length_dev, head_share, P_SIZE)
    gk = got[:, rows : 2 * rows].reshape(lo_count, length_dev, head_share, P_SIZE)
    base = 2 * rows
    bk = got[:, base : base + length_dev]
    ck = got[:, base + length_dev : base + 2 * length_dev]
    base = base + 2 * length_dev
    deck = got[:, base : base + head_share]
    flk = got[:, base + head_share]
    gain = lax.dynamic_slice_in_dim(skip[0], first_head, head_share)

    parts, through, block_end, block_start = local_terms(xk, gk, bk, ck, deck, flk)

    entering_block = jnp.zeros_like(block_end)
    leaving_block = jnp.zeros_like(block_start)
    for _ in range(hi_count - 1):
        entering_block = from_behind(through[:, None, None] * entering_block + block_end, "hi", 1)
        leaving_block = from_behind(through[:, None, None] * leaving_block + block_start, "hi", -1)

    mixed, grads = finish(parts, xk, gk, bk, ck, gain, entering_block, leaving_block)
    homeward = jnp.concatenate(
        [mixed.reshape(lo_count, rows, 128), grads.reshape(lo_count, rows, 128)], axis=1
    ).astype(BF16)
    back = lax.all_to_all(homeward, "lo", split_axis=0, concat_axis=0, tiled=True)

    def from_rows(value):
        return value.reshape(lo_count, length_dev, lanes).transpose(1, 0, 2).reshape(
            1, length_dev, local_heads * P_SIZE
        )

    return (from_rows(back[:, :rows]), from_rows(back[:, rows:]))


def solution(mesh):
    pipe_count, seq_count, tp_count = mesh.devices.shape
    split_mesh = Mesh(
        mesh.devices.reshape(pipe_count, seq_count // LOCAL, LOCAL, tp_count),
        ("pipe", "hi", "lo", "tp"),
    )
    placed = (
        P("pipe", SEQ, "tp"),
        P("pipe", SEQ, "tp"),
        P("pipe", SEQ, "tp"),
        P("pipe", SEQ, "tp"),
        P("pipe", SEQ, "tp"),
        P("pipe", SEQ),
        P("pipe", "tp"),
    )
    return jax.shard_map(
        body,
        mesh=split_mesh,
        in_specs=placed,
        out_specs=(P("pipe", SEQ, "tp"), P("pipe", SEQ, "tp")),
        check_vma=False,
    )
```

```python
import jax
import jax.numpy as jnp
from jax import lax
from jax.sharding import Mesh
from jax.sharding import PartitionSpec as P

BLEND_CHANNELS = 128
P_SIZE = 64
N = 128
GROUPS = 4
MISC = 16
LOCAL = 4
PIECES = 2

F32 = jnp.float32
BF16 = jnp.bfloat16
HIGH = lax.Precision.HIGHEST
SEQ = ("hi", "lo")


def from_behind(value, axis, steps):
    count = lax.axis_size(axis)
    leading, last = (max(0, -steps), min(count, count - steps))
    return lax.ppermute(value, axis, [(source, source + steps) for source in range(leading, last)])


def mm(spec, a, b):
    return jnp.einsum(spec, a, b, preferred_element_type=F32)


def mm_wide(spec, a, b):
    return jnp.einsum(spec, a.astype(F32), b.astype(F32), precision=HIGH)


def local_terms(xk, gk, bk, ck, deck, flk):
    chunks, width = flk.shape
    order = jnp.arange(width)
    causal = order[:, None] >= order[None, :]
    tri = causal.astype(BF16)
    cum = mm("tu,khu->kht", tri, deck)
    seg = mm("tu,ku->kt", tri, flk)

    cum_end = cum[:, :, -1]
    seg_end = seg[:, -1]
    outflow = jnp.exp(cum_end[:, :, None] - cum) * (seg == seg_end[:, None])[:, None, :]
    inflow = jnp.exp(cum) * (seg == 0.0)[:, None, :]
    outflow_q = outflow.transpose(0, 2, 1)[..., None]
    inflow_q = inflow.transpose(0, 2, 1)[..., None]
    end_states = mm_wide("kun,kuhp->khnp", bk, outflow_q * xk.astype(F32))
    start_states = mm_wide("ktn,kthp->khnp", ck, inflow_q * gk.astype(F32))

    total = jnp.cumsum(cum_end, axis=0)
    opened = jnp.cumsum((seg_end > 0.0).astype(F32))
    total_prev = jnp.concatenate([jnp.zeros_like(total[:1]), total[:-1]], axis=0)
    opened_prev = jnp.concatenate([jnp.zeros_like(opened[:1]), opened[:-1]], axis=0)
    index = jnp.arange(chunks)
    reach = (index[None, :] < index[:, None]) & (opened_prev[:, None] == opened[None, :])
    carry = jnp.where(
        reach[:, :, None],
        jnp.exp(jnp.minimum(total_prev[:, None, :] - total[None, :, :], 0.0)),
        0.0,
    )
    from_start = jnp.exp(total_prev) * (opened_prev == 0.0)[:, None]
    to_end = jnp.exp(jnp.minimum(total[-1][None, :] - total, 0.0)) * (opened == opened[-1])[:, None]
    through = jnp.exp(total[-1]) * (opened[-1] == 0.0)
    block_end = jnp.einsum("kh,khnp->hnp", to_end, end_states, precision=HIGH)
    block_start = jnp.einsum("kh,khnp->hnp", from_start, start_states, precision=HIGH)
    parts = dict(
        cum=cum, seg=seg, causal=causal, inflow_q=inflow_q, outflow_q=outflow_q,
        end_states=end_states, start_states=start_states, carry=carry,
        from_start=from_start, to_end=to_end,
    )
    return parts, through, block_end, block_start


def finish(parts, xk, gk, bk, ck, gain, entering_block, leaving_block):
    cum, seg, causal = parts["cum"], parts["seg"], parts["causal"]
    linked = (seg[:, :, None] == seg[:, None, :]) & causal[None]
    spread = cum[:, :, :, None] - cum[:, :, None, :]
    damping = jnp.where(linked[:, None], jnp.exp(jnp.minimum(spread, 0.0)), 0.0)
    overlap = mm("ktn,kun->ktu", ck, bk)
    mixing = damping * overlap[:, None]
    mixed = mm_wide("khtu,kuhp->kthp", mixing, xk)
    grads = mm_wide("khtu,kthp->kuhp", mixing, gk)

    carry = parts["carry"]
    entering = jnp.einsum("kjh,jhnp->khnp", carry, parts["end_states"], precision=HIGH)
    leaving = jnp.einsum("jkh,jhnp->khnp", carry, parts["start_states"], precision=HIGH)
    entering = entering + parts["from_start"][:, :, None, None] * entering_block[None]
    leaving = leaving + parts["to_end"][:, :, None, None] * leaving_block[None]

    mixed = mixed + parts["inflow_q"] * mm_wide("ktn,khnp->kthp", ck, entering)
    grads = grads + parts["outflow_q"] * mm_wide("kun,khnp->kuhp", bk, leaving)
    gain_wide = gain[None, None, :, None]
    mixed = mixed + gain_wide * xk.astype(F32)
    grads = grads + gain_wide * gk.astype(F32)
    return mixed, grads


def chain(block, through, count, steps):
    pieces = []
    width = block.shape[0] // PIECES
    for piece in range(PIECES):
        own = block[piece * width : (piece + 1) * width]
        gain = through[piece * width : (piece + 1) * width, None, None]
        state = jnp.zeros_like(own)
        for _ in range(count - 1):
            state = from_behind(gain * state + own, "hi", steps)
        pieces.append(state)
    return jnp.concatenate(pieces, axis=0)


def body(emitted, cotangent, b_proj, c_proj, log_decay, starts, skip):
    shifted = from_behind(emitted, "pipe", 1)
    inputs = jnp.where(lax.axis_index("pipe") == 0, emitted, shifted)[0]
    upstream = cotangent[0]
    length_dev = inputs.shape[0]
    lo_count = lax.axis_size("lo")
    hi_count = lax.axis_size("hi")
    local_heads = skip.shape[1]
    head_share = local_heads // lo_count
    lanes = head_share * P_SIZE
    rows = lanes * length_dev // 128
    lo_pos = lax.axis_index("lo")
    first_head = lo_pos * head_share

    def to_rows(value):
        return value.reshape(length_dev, lo_count, lanes).transpose(1, 0, 2).reshape(lo_count, rows, 128)

    decay_rows = log_decay[0].reshape(length_dev, lo_count, head_share).transpose(1, 2, 0)
    flag_rows = jnp.broadcast_to(starts[0].astype(BF16)[None, None, :], (lo_count, 1, length_dev))
    proj = jnp.concatenate([b_proj[0], c_proj[0]], axis=0)
    proj_rows = jnp.broadcast_to(proj[None], (lo_count,) + proj.shape)
    filler = jnp.zeros((lo_count, MISC - head_share - 1, length_dev), BF16)
    payload = jnp.concatenate(
        [to_rows(inputs), to_rows(upstream), proj_rows, decay_rows, flag_rows, filler], axis=1
    )
    got = lax.all_to_all(payload, "lo", split_axis=0, concat_axis=0, tiled=True)

    xk = got[:, :rows].reshape(lo_count, length_dev, head_share, P_SIZE)
    gk = got[:, rows : 2 * rows].reshape(lo_count, length_dev, head_share, P_SIZE)
    base = 2 * rows
    bk = got[:, base : base + length_dev]
    ck = got[:, base + length_dev : base + 2 * length_dev]
    base = base + 2 * length_dev
    deck = got[:, base : base + head_share]
    flk = got[:, base + head_share]
    gain = lax.dynamic_slice_in_dim(skip[0], first_head, head_share)

    parts, through, block_end, block_start = local_terms(xk, gk, bk, ck, deck, flk)

    entering_block = chain(block_end, through, hi_count, 1)
    leaving_block = chain(block_start, through, hi_count, -1)

    mixed, grads = finish(parts, xk, gk, bk, ck, gain, entering_block, leaving_block)
    homeward = jnp.concatenate(
        [mixed.reshape(lo_count, rows, 128), grads.reshape(lo_count, rows, 128)], axis=1
    ).astype(BF16)
    back = lax.all_to_all(homeward, "lo", split_axis=0, concat_axis=0, tiled=True)

    def from_rows(value):
        return value.reshape(lo_count, length_dev, lanes).transpose(1, 0, 2).reshape(
            1, length_dev, local_heads * P_SIZE
        )

    return (from_rows(back[:, :rows]), from_rows(back[:, rows:]))


def solution(mesh):
    pipe_count, seq_count, tp_count = mesh.devices.shape
    split_mesh = Mesh(
        mesh.devices.reshape(pipe_count, seq_count // LOCAL, LOCAL, tp_count),
        ("pipe", "hi", "lo", "tp"),
    )
    placed = (
        P("pipe", SEQ, "tp"),
        P("pipe", SEQ, "tp"),
        P("pipe", SEQ, "tp"),
        P("pipe", SEQ, "tp"),
        P("pipe", SEQ, "tp"),
        P("pipe", SEQ),
        P("pipe", "tp"),
    )
    return jax.shard_map(
        body,
        mesh=split_mesh,
        in_specs=placed,
        out_specs=(P("pipe", SEQ, "tp"), P("pipe", SEQ, "tp")),
        check_vma=False,
    )
```

```python
import jax
import jax.numpy as jnp
from jax import lax
from jax.sharding import Mesh
from jax.sharding import PartitionSpec as P

BLEND_CHANNELS = 128
P_SIZE = 64
N = 128
GROUPS = 4
MISC = 16
LOCAL = 4

F32 = jnp.float32
BF16 = jnp.bfloat16
HIGH = lax.Precision.HIGHEST
SEQ = ("hi", "lo")


def from_behind(value, axis, steps):
    count = lax.axis_size(axis)
    leading, last = (max(0, -steps), min(count, count - steps))
    return lax.ppermute(value, axis, [(source, source + steps) for source in range(leading, last)])


def mm(spec, a, b):
    return jnp.einsum(spec, a, b, preferred_element_type=F32)


def mm_wide(spec, a, b):
    return jnp.einsum(spec, a.astype(F32), b.astype(F32), precision=HIGH)


def local_terms(xk, gk, bk, ck, deck, flk):
    chunks, width = flk.shape
    order = jnp.arange(width)
    causal = order[:, None] >= order[None, :]
    tri = causal.astype(BF16)
    cum = mm("tu,khu->kht", tri, deck)
    seg = mm("tu,ku->kt", tri, flk)

    cum_end = cum[:, :, -1]
    seg_end = seg[:, -1]
    outflow = jnp.exp(cum_end[:, :, None] - cum) * (seg == seg_end[:, None])[:, None, :]
    inflow = jnp.exp(cum) * (seg == 0.0)[:, None, :]
    outflow_q = outflow.transpose(0, 2, 1)[..., None]
    inflow_q = inflow.transpose(0, 2, 1)[..., None]
    end_states = mm_wide("kun,kuhp->khnp", bk, outflow_q * xk.astype(F32))
    start_states = mm_wide("ktn,kthp->khnp", ck, inflow_q * gk.astype(F32))

    total = jnp.cumsum(cum_end, axis=0)
    opened = jnp.cumsum((seg_end > 0.0).astype(F32))
    total_prev = jnp.concatenate([jnp.zeros_like(total[:1]), total[:-1]], axis=0)
    opened_prev = jnp.concatenate([jnp.zeros_like(opened[:1]), opened[:-1]], axis=0)
    index = jnp.arange(chunks)
    reach = (index[None, :] < index[:, None]) & (opened_prev[:, None] == opened[None, :])
    carry = jnp.where(
        reach[:, :, None],
        jnp.exp(jnp.minimum(total_prev[:, None, :] - total[None, :, :], 0.0)),
        0.0,
    )
    from_start = jnp.exp(total_prev) * (opened_prev == 0.0)[:, None]
    to_end = jnp.exp(jnp.minimum(total[-1][None, :] - total, 0.0)) * (opened == opened[-1])[:, None]
    through = jnp.exp(total[-1]) * (opened[-1] == 0.0)
    block_end = jnp.einsum("kh,khnp->hnp", to_end, end_states, precision=HIGH)
    block_start = jnp.einsum("kh,khnp->hnp", from_start, start_states, precision=HIGH)
    parts = dict(
        cum=cum, seg=seg, causal=causal, inflow_q=inflow_q, outflow_q=outflow_q,
        end_states=end_states, start_states=start_states, carry=carry,
        from_start=from_start, to_end=to_end,
    )
    return parts, through, block_end, block_start


def finish(parts, xk, gk, bk, ck, gain, entering_block, leaving_block):
    cum, seg, causal = parts["cum"], parts["seg"], parts["causal"]
    linked = (seg[:, :, None] == seg[:, None, :]) & causal[None]
    spread = cum[:, :, :, None] - cum[:, :, None, :]
    damping = jnp.where(linked[:, None], jnp.exp(jnp.minimum(spread, 0.0)), 0.0)
    overlap = mm("ktn,kun->ktu", ck, bk)
    mixing = damping * overlap[:, None]
    mixed = mm_wide("khtu,kuhp->kthp", mixing, xk)
    grads = mm_wide("khtu,kthp->kuhp", mixing, gk)

    carry = parts["carry"]
    entering = jnp.einsum("kjh,jhnp->khnp", carry, parts["end_states"], precision=HIGH)
    leaving = jnp.einsum("jkh,jhnp->khnp", carry, parts["start_states"], precision=HIGH)
    entering = entering + parts["from_start"][:, :, None, None] * entering_block[None]
    leaving = leaving + parts["to_end"][:, :, None, None] * leaving_block[None]

    mixed = mixed + parts["inflow_q"] * mm_wide("ktn,khnp->kthp", ck, entering)
    grads = grads + parts["outflow_q"] * mm_wide("kun,khnp->kuhp", bk, leaving)
    gain_wide = gain[None, None, :, None]
    mixed = mixed + gain_wide * xk.astype(F32)
    grads = grads + gain_wide * gk.astype(F32)
    return mixed, grads


def pack(state, gain):
    heads, rows, width = state.shape
    corner = (jnp.arange(8)[:, None] == 0) & (jnp.arange(width)[None, :] == 0)
    tail = gain[:, None, None] * corner[None].astype(F32)
    return jnp.concatenate([state, tail], axis=1)


def scan_four(block, through, steps):
    rows = block.shape[1]
    first = from_behind(pack(block, through), "hi", steps)
    prev_state = first[:, :rows]
    inclusive = through[:, None, None] * prev_state + block
    far = through[:, None, None] * prev_state
    near = from_behind(pack(inclusive, through), "hi", steps)
    farther = from_behind(far, "hi", 2 * steps)
    return near[:, :rows] + near[:, rows, 0][:, None, None] * farther


def body(emitted, cotangent, b_proj, c_proj, log_decay, starts, skip):
    shifted = from_behind(emitted, "pipe", 1)
    inputs = jnp.where(lax.axis_index("pipe") == 0, emitted, shifted)[0]
    upstream = cotangent[0]
    length_dev = inputs.shape[0]
    lo_count = lax.axis_size("lo")
    hi_count = lax.axis_size("hi")
    local_heads = skip.shape[1]
    head_share = local_heads // lo_count
    lanes = head_share * P_SIZE
    rows = lanes * length_dev // 128
    lo_pos = lax.axis_index("lo")
    first_head = lo_pos * head_share

    def to_rows(value):
        return value.reshape(length_dev, lo_count, lanes).transpose(1, 0, 2).reshape(lo_count, rows, 128)

    decay_rows = log_decay[0].reshape(length_dev, lo_count, head_share).transpose(1, 2, 0)
    flag_rows = jnp.broadcast_to(starts[0].astype(BF16)[None, None, :], (lo_count, 1, length_dev))
    proj = jnp.concatenate([b_proj[0], c_proj[0]], axis=0)
    proj_rows = jnp.broadcast_to(proj[None], (lo_count,) + proj.shape)
    filler = jnp.zeros((lo_count, MISC - head_share - 1, length_dev), BF16)
    payload = jnp.concatenate(
        [to_rows(inputs), to_rows(upstream), proj_rows, decay_rows, flag_rows, filler], axis=1
    )
    got = lax.all_to_all(payload, "lo", split_axis=0, concat_axis=0, tiled=True)

    xk = got[:, :rows].reshape(lo_count, length_dev, head_share, P_SIZE)
    gk = got[:, rows : 2 * rows].reshape(lo_count, length_dev, head_share, P_SIZE)
    base = 2 * rows
    bk = got[:, base : base + length_dev]
    ck = got[:, base + length_dev : base + 2 * length_dev]
    base = base + 2 * length_dev
    deck = got[:, base : base + head_share]
    flk = got[:, base + head_share]
    gain = lax.dynamic_slice_in_dim(skip[0], first_head, head_share)

    parts, through, block_end, block_start = local_terms(xk, gk, bk, ck, deck, flk)

    if hi_count == 4:
        entering_block = scan_four(block_end, through, 1)
        leaving_block = scan_four(block_start, through, -1)
    else:
        entering_block = jnp.zeros_like(block_end)
        leaving_block = jnp.zeros_like(block_start)
        for _ in range(hi_count - 1):
            entering_block = from_behind(through[:, None, None] * entering_block + block_end, "hi", 1)
            leaving_block = from_behind(through[:, None, None] * leaving_block + block_start, "hi", -1)

    mixed, grads = finish(parts, xk, gk, bk, ck, gain, entering_block, leaving_block)
    homeward = jnp.concatenate(
        [mixed.reshape(lo_count, rows, 128), grads.reshape(lo_count, rows, 128)], axis=1
    ).astype(BF16)
    back = lax.all_to_all(homeward, "lo", split_axis=0, concat_axis=0, tiled=True)

    def from_rows(value):
        return value.reshape(lo_count, length_dev, lanes).transpose(1, 0, 2).reshape(
            1, length_dev, local_heads * P_SIZE
        )

    return (from_rows(back[:, :rows]), from_rows(back[:, rows:]))


def solution(mesh):
    pipe_count, seq_count, tp_count = mesh.devices.shape
    split_mesh = Mesh(
        mesh.devices.reshape(pipe_count, seq_count // LOCAL, LOCAL, tp_count),
        ("pipe", "hi", "lo", "tp"),
    )
    placed = (
        P("pipe", SEQ, "tp"),
        P("pipe", SEQ, "tp"),
        P("pipe", SEQ, "tp"),
        P("pipe", SEQ, "tp"),
        P("pipe", SEQ, "tp"),
        P("pipe", SEQ),
        P("pipe", "tp"),
    )
    return jax.shard_map(
        body,
        mesh=split_mesh,
        in_specs=placed,
        out_specs=(P("pipe", SEQ, "tp"), P("pipe", SEQ, "tp")),
        check_vma=False,
    )
```

```python
import jax
import jax.numpy as jnp
from jax import lax
from jax.sharding import Mesh
from jax.sharding import PartitionSpec as P

BLEND_CHANNELS = 128
P_SIZE = 64
N = 128
GROUPS = 4
MISC = 16
LOCAL = 4

F32 = jnp.float32
BF16 = jnp.bfloat16
HIGH = lax.Precision.HIGHEST
SEQ = ("hi", "lo")


def from_behind(value, axis, steps):
    count = lax.axis_size(axis)
    leading, last = (max(0, -steps), min(count, count - steps))
    return lax.ppermute(value, axis, [(source, source + steps) for source in range(leading, last)])


def mm(spec, a, b):
    return jnp.einsum(spec, a, b, preferred_element_type=F32)


def mm_wide(spec, a, b):
    return jnp.einsum(spec, a.astype(F32), b.astype(F32), precision=HIGH)


def local_terms(xk, gk, bk, ck, deck, flk):
    chunks, width = flk.shape
    order = jnp.arange(width)
    causal = order[:, None] >= order[None, :]
    tri = causal.astype(BF16)
    cum = mm("tu,khu->kht", tri, deck)
    seg = mm("tu,ku->kt", tri, flk)

    cum_end = cum[:, :, -1]
    seg_end = seg[:, -1]
    outflow = jnp.exp(cum_end[:, :, None] - cum) * (seg == seg_end[:, None])[:, None, :]
    inflow = jnp.exp(cum) * (seg == 0.0)[:, None, :]
    outflow_q = outflow.transpose(0, 2, 1)[..., None]
    inflow_q = inflow.transpose(0, 2, 1)[..., None]
    end_states = mm_wide("kun,kuhp->khnp", bk, outflow_q * xk.astype(F32))
    start_states = mm_wide("ktn,kthp->khnp", ck, inflow_q * gk.astype(F32))

    total = jnp.cumsum(cum_end, axis=0)
    opened = jnp.cumsum((seg_end > 0.0).astype(F32))
    total_prev = jnp.concatenate([jnp.zeros_like(total[:1]), total[:-1]], axis=0)
    opened_prev = jnp.concatenate([jnp.zeros_like(opened[:1]), opened[:-1]], axis=0)
    index = jnp.arange(chunks)
    reach = (index[None, :] < index[:, None]) & (opened_prev[:, None] == opened[None, :])
    carry = jnp.where(
        reach[:, :, None],
        jnp.exp(jnp.minimum(total_prev[:, None, :] - total[None, :, :], 0.0)),
        0.0,
    )
    from_start = jnp.exp(total_prev) * (opened_prev == 0.0)[:, None]
    to_end = jnp.exp(jnp.minimum(total[-1][None, :] - total, 0.0)) * (opened == opened[-1])[:, None]
    through = jnp.exp(total[-1]) * (opened[-1] == 0.0)
    block_end = jnp.einsum("kh,khnp->hnp", to_end, end_states, precision=HIGH)
    block_start = jnp.einsum("kh,khnp->hnp", from_start, start_states, precision=HIGH)
    parts = dict(
        cum=cum, seg=seg, causal=causal, inflow_q=inflow_q, outflow_q=outflow_q,
        end_states=end_states, start_states=start_states, carry=carry,
        from_start=from_start, to_end=to_end,
    )
    return parts, through, block_end, block_start


def finish_local(parts, xk, gk, bk, ck, gain):
    cum, seg, causal = parts["cum"], parts["seg"], parts["causal"]
    linked = (seg[:, :, None] == seg[:, None, :]) & causal[None]
    spread = cum[:, :, :, None] - cum[:, :, None, :]
    damping = jnp.where(linked[:, None], jnp.exp(jnp.minimum(spread, 0.0)), 0.0)
    overlap = mm("ktn,kun->ktu", ck, bk)
    mixing = damping * overlap[:, None]
    mixed = mm_wide("khtu,kuhp->kthp", mixing, xk)
    grads = mm_wide("khtu,kthp->kuhp", mixing, gk)

    carry = parts["carry"]
    entering = jnp.einsum("kjh,jhnp->khnp", carry, parts["end_states"], precision=HIGH)
    leaving = jnp.einsum("jkh,jhnp->khnp", carry, parts["start_states"], precision=HIGH)
    mixed = mixed + parts["inflow_q"] * mm_wide("ktn,khnp->kthp", ck, entering)
    grads = grads + parts["outflow_q"] * mm_wide("kun,khnp->kuhp", bk, leaving)
    gain_wide = gain[None, None, :, None]
    mixed = mixed + gain_wide * xk.astype(F32)
    grads = grads + gain_wide * gk.astype(F32)
    return mixed, grads


def finish_outer(parts, mixed, grads, bk, ck, entering_block, leaving_block):
    entering_rows = mm_wide("ktn,hnp->kthp", ck, entering_block)
    leaving_rows = mm_wide("kun,hnp->kuhp", bk, leaving_block)
    from_start = parts["from_start"][:, None, :, None]
    to_end = parts["to_end"][:, None, :, None]
    mixed = mixed + parts["inflow_q"] * (from_start * entering_rows)
    grads = grads + parts["outflow_q"] * (to_end * leaving_rows)
    return mixed, grads


def body(emitted, cotangent, b_proj, c_proj, log_decay, starts, skip):
    shifted = from_behind(emitted, "pipe", 1)
    inputs = jnp.where(lax.axis_index("pipe") == 0, emitted, shifted)[0]
    upstream = cotangent[0]
    length_dev = inputs.shape[0]
    lo_count = lax.axis_size("lo")
    hi_count = lax.axis_size("hi")
    local_heads = skip.shape[1]
    head_share = local_heads // lo_count
    lanes = head_share * P_SIZE
    rows = lanes * length_dev // 128
    lo_pos = lax.axis_index("lo")
    first_head = lo_pos * head_share

    def to_rows(value):
        return value.reshape(length_dev, lo_count, lanes).transpose(1, 0, 2).reshape(lo_count, rows, 128)

    decay_rows = log_decay[0].reshape(length_dev, lo_count, head_share).transpose(1, 2, 0)
    flag_rows = jnp.broadcast_to(starts[0].astype(BF16)[None, None, :], (lo_count, 1, length_dev))
    proj = jnp.concatenate([b_proj[0], c_proj[0]], axis=0)
    proj_rows = jnp.broadcast_to(proj[None], (lo_count,) + proj.shape)
    filler = jnp.zeros((lo_count, MISC - head_share - 1, length_dev), BF16)
    payload = jnp.concatenate(
        [to_rows(inputs), to_rows(upstream), proj_rows, decay_rows, flag_rows, filler], axis=1
    )
    got = lax.all_to_all(payload, "lo", split_axis=0, concat_axis=0, tiled=True)

    xk = got[:, :rows].reshape(lo_count, length_dev, head_share, P_SIZE)
    gk = got[:, rows : 2 * rows].reshape(lo_count, length_dev, head_share, P_SIZE)
    base = 2 * rows
    bk = got[:, base : base + length_dev]
    ck = got[:, base + length_dev : base + 2 * length_dev]
    base = base + 2 * length_dev
    deck = got[:, base : base + head_share]
    flk = got[:, base + head_share]
    gain = lax.dynamic_slice_in_dim(skip[0], first_head, head_share)

    parts, through, block_end, block_start = local_terms(xk, gk, bk, ck, deck, flk)
    mixed, grads = finish_local(parts, xk, gk, bk, ck, gain)
    block_end, block_start, mixed, grads = lax.optimization_barrier(
        (block_end, block_start, mixed, grads)
    )

    entering_block = jnp.zeros_like(block_end)
    leaving_block = jnp.zeros_like(block_start)
    for _ in range(hi_count - 1):
        entering_block = from_behind(through[:, None, None] * entering_block + block_end, "hi", 1)
        leaving_block = from_behind(through[:, None, None] * leaving_block + block_start, "hi", -1)

    mixed, grads = finish_outer(parts, mixed, grads, bk, ck, entering_block, leaving_block)
    homeward = jnp.concatenate(
        [mixed.reshape(lo_count, rows, 128), grads.reshape(lo_count, rows, 128)], axis=1
    ).astype(BF16)
    back = lax.all_to_all(homeward, "lo", split_axis=0, concat_axis=0, tiled=True)

    def from_rows(value):
        return value.reshape(lo_count, length_dev, lanes).transpose(1, 0, 2).reshape(
            1, length_dev, local_heads * P_SIZE
        )

    return (from_rows(back[:, :rows]), from_rows(back[:, rows:]))


def solution(mesh):
    pipe_count, seq_count, tp_count = mesh.devices.shape
    split_mesh = Mesh(
        mesh.devices.reshape(pipe_count, seq_count // LOCAL, LOCAL, tp_count),
        ("pipe", "hi", "lo", "tp"),
    )
    placed = (
        P("pipe", SEQ, "tp"),
        P("pipe", SEQ, "tp"),
        P("pipe", SEQ, "tp"),
        P("pipe", SEQ, "tp"),
        P("pipe", SEQ, "tp"),
        P("pipe", SEQ),
        P("pipe", "tp"),
    )
    return jax.shard_map(
        body,
        mesh=split_mesh,
        in_specs=placed,
        out_specs=(P("pipe", SEQ, "tp"), P("pipe", SEQ, "tp")),
        check_vma=False,
    )
```

```python
import jax
import jax.numpy as jnp
from jax import lax
from jax.sharding import Mesh
from jax.sharding import PartitionSpec as P

BLEND_CHANNELS = 128
P_SIZE = 64
N = 128
GROUPS = 4
MISC = 16
LOCAL = 4

F32 = jnp.float32
BF16 = jnp.bfloat16
HIGH = lax.Precision.HIGHEST
SEQ = ("hi", "lo")


def from_behind(value, axis, steps):
    count = lax.axis_size(axis)
    leading, last = (max(0, -steps), min(count, count - steps))
    return lax.ppermute(value, axis, [(source, source + steps) for source in range(leading, last)])


def ring_shift(value, axis, steps):
    count = lax.axis_size(axis)
    return lax.ppermute(value, axis, [(source, (source + steps) % count) for source in range(count)])


def mm(spec, a, b):
    return jnp.einsum(spec, a, b, preferred_element_type=F32)


def mm_wide(spec, a, b):
    return jnp.einsum(spec, a.astype(F32), b.astype(F32), precision=HIGH)


def local_terms(xk, gk, bk, ck, deck, flk):
    chunks, width = flk.shape
    order = jnp.arange(width)
    causal = order[:, None] >= order[None, :]
    tri = causal.astype(BF16)
    cum = mm("tu,khu->kht", tri, deck)
    seg = mm("tu,ku->kt", tri, flk)

    cum_end = cum[:, :, -1]
    seg_end = seg[:, -1]
    outflow = jnp.exp(cum_end[:, :, None] - cum) * (seg == seg_end[:, None])[:, None, :]
    inflow = jnp.exp(cum) * (seg == 0.0)[:, None, :]
    outflow_q = outflow.transpose(0, 2, 1)[..., None]
    inflow_q = inflow.transpose(0, 2, 1)[..., None]
    end_states = mm_wide("kun,kuhp->khnp", bk, outflow_q * xk.astype(F32))
    start_states = mm_wide("ktn,kthp->khnp", ck, inflow_q * gk.astype(F32))

    total = jnp.cumsum(cum_end, axis=0)
    opened = jnp.cumsum((seg_end > 0.0).astype(F32))
    total_prev = jnp.concatenate([jnp.zeros_like(total[:1]), total[:-1]], axis=0)
    opened_prev = jnp.concatenate([jnp.zeros_like(opened[:1]), opened[:-1]], axis=0)
    index = jnp.arange(chunks)
    reach = (index[None, :] < index[:, None]) & (opened_prev[:, None] == opened[None, :])
    carry = jnp.where(
        reach[:, :, None],
        jnp.exp(jnp.minimum(total_prev[:, None, :] - total[None, :, :], 0.0)),
        0.0,
    )
    from_start = jnp.exp(total_prev) * (opened_prev == 0.0)[:, None]
    to_end = jnp.exp(jnp.minimum(total[-1][None, :] - total, 0.0)) * (opened == opened[-1])[:, None]
    through = jnp.exp(total[-1]) * (opened[-1] == 0.0)
    block_end = jnp.einsum("kh,khnp->hnp", to_end, end_states, precision=HIGH)
    block_start = jnp.einsum("kh,khnp->hnp", from_start, start_states, precision=HIGH)
    parts = dict(
        cum=cum, seg=seg, causal=causal, inflow_q=inflow_q, outflow_q=outflow_q,
        end_states=end_states, start_states=start_states, carry=carry,
        from_start=from_start, to_end=to_end,
    )
    return parts, through, block_end, block_start


def finish(parts, xk, gk, bk, ck, gain, entering_block, leaving_block):
    cum, seg, causal = parts["cum"], parts["seg"], parts["causal"]
    linked = (seg[:, :, None] == seg[:, None, :]) & causal[None]
    spread = cum[:, :, :, None] - cum[:, :, None, :]
    damping = jnp.where(linked[:, None], jnp.exp(jnp.minimum(spread, 0.0)), 0.0)
    overlap = mm("ktn,kun->ktu", ck, bk)
    mixing = damping * overlap[:, None]
    mixed = mm_wide("khtu,kuhp->kthp", mixing, xk)
    grads = mm_wide("khtu,kthp->kuhp", mixing, gk)

    carry = parts["carry"]
    entering = jnp.einsum("kjh,jhnp->khnp", carry, parts["end_states"], precision=HIGH)
    leaving = jnp.einsum("jkh,jhnp->khnp", carry, parts["start_states"], precision=HIGH)
    entering = entering + parts["from_start"][:, :, None, None] * entering_block[None]
    leaving = leaving + parts["to_end"][:, :, None, None] * leaving_block[None]

    mixed = mixed + parts["inflow_q"] * mm_wide("ktn,khnp->kthp", ck, entering)
    grads = grads + parts["outflow_q"] * mm_wide("kun,khnp->kuhp", bk, leaving)
    gain_wide = gain[None, None, :, None]
    mixed = mixed + gain_wide * xk.astype(F32)
    grads = grads + gain_wide * gk.astype(F32)
    return mixed, grads


def body(emitted, cotangent, b_proj, c_proj, log_decay, starts, skip):
    shifted = from_behind(emitted, "pipe", 1)
    inputs = jnp.where(lax.axis_index("pipe") == 0, emitted, shifted)[0]
    upstream = cotangent[0]
    length_dev = inputs.shape[0]
    lo_count = lax.axis_size("lo")
    hi_count = lax.axis_size("hi")
    local_heads = skip.shape[1]
    head_share = local_heads // lo_count
    lanes = head_share * P_SIZE
    rows = lanes * length_dev // 128
    lo_pos = lax.axis_index("lo")
    first_head = lo_pos * head_share

    def to_rows(value):
        return value.reshape(length_dev, lo_count, lanes).transpose(1, 0, 2).reshape(lo_count, rows, 128)

    decay_rows = log_decay[0].reshape(length_dev, lo_count, head_share).transpose(1, 2, 0)
    flag_rows = jnp.broadcast_to(starts[0].astype(BF16)[None, None, :], (lo_count, 1, length_dev))
    proj = jnp.concatenate([b_proj[0], c_proj[0]], axis=0)
    proj_rows = jnp.broadcast_to(proj[None], (lo_count,) + proj.shape)
    filler = jnp.zeros((lo_count, MISC - head_share - 1, length_dev), BF16)
    payload = jnp.concatenate(
        [to_rows(inputs), to_rows(upstream), proj_rows, decay_rows, flag_rows, filler], axis=1
    )
    got = lax.all_to_all(payload, "lo", split_axis=0, concat_axis=0, tiled=True)

    xk = got[:, :rows].reshape(lo_count, length_dev, head_share, P_SIZE)
    gk = got[:, rows : 2 * rows].reshape(lo_count, length_dev, head_share, P_SIZE)
    base = 2 * rows
    bk = got[:, base : base + length_dev]
    ck = got[:, base + length_dev : base + 2 * length_dev]
    base = base + 2 * length_dev
    deck = got[:, base : base + head_share]
    flk = got[:, base + head_share]
    gain = lax.dynamic_slice_in_dim(skip[0], first_head, head_share)

    parts, through, block_end, block_start = local_terms(xk, gk, bk, ck, deck, flk)

    entering_block = jnp.zeros_like(block_end)
    leaving_block = jnp.zeros_like(block_start)
    hi_pos = lax.axis_index("hi")
    for _ in range(hi_count - 1):
        entering_block = jnp.where(
            hi_pos == 0, 0.0, ring_shift(through[:, None, None] * entering_block + block_end, "hi", 1)
        )
        leaving_block = jnp.where(
            hi_pos == hi_count - 1,
            0.0,
            ring_shift(through[:, None, None] * leaving_block + block_start, "hi", -1),
        )

    mixed, grads = finish(parts, xk, gk, bk, ck, gain, entering_block, leaving_block)
    homeward = jnp.concatenate(
        [mixed.reshape(lo_count, rows, 128), grads.reshape(lo_count, rows, 128)], axis=1
    ).astype(BF16)
    back = lax.all_to_all(homeward, "lo", split_axis=0, concat_axis=0, tiled=True)

    def from_rows(value):
        return value.reshape(lo_count, length_dev, lanes).transpose(1, 0, 2).reshape(
            1, length_dev, local_heads * P_SIZE
        )

    return (from_rows(back[:, :rows]), from_rows(back[:, rows:]))


def solution(mesh):
    pipe_count, seq_count, tp_count = mesh.devices.shape
    split_mesh = Mesh(
        mesh.devices.reshape(pipe_count, seq_count // LOCAL, LOCAL, tp_count),
        ("pipe", "hi", "lo", "tp"),
    )
    placed = (
        P("pipe", SEQ, "tp"),
        P("pipe", SEQ, "tp"),
        P("pipe", SEQ, "tp"),
        P("pipe", SEQ, "tp"),
        P("pipe", SEQ, "tp"),
        P("pipe", SEQ),
        P("pipe", "tp"),
    )
    return jax.shard_map(
        body,
        mesh=split_mesh,
        in_specs=placed,
        out_specs=(P("pipe", SEQ, "tp"), P("pipe", SEQ, "tp")),
        check_vma=False,
    )
```
